768 devices in a mesh: ctx: 64 (over x, y, core), head: 12 (over z).
Axes of the slice: x: 4, y: 8, z: 12, core: 2. Of those that a mesh axis runs over, the one named last changes fastest.
Arguments:
- queries: bfloat16 [24576, 3072], P('ctx', 'head'), may hold values from -6 to 6, as said below
- keys: bfloat16 [24576, 3072], P('ctx', 'head'), may hold values from -6 to 6, as said below
- values: bfloat16 [24576, 3072], P('ctx', 'head'), may hold values from -6 to 6
- out_weight: bfloat16 [3072, 4096], P('head'), may hold values from -0.109375 to 0.109375
Outputs:
- mixed: bfloat16 [24576, 4096], P(('ctx', 'head'))
The draws below stay inside these ranges and needn't reach their ends.
Inputs may be any that keep to these rules, and one draw needn't show every extreme that they name: `queries`: entries of order one. `keys`: entries of order one.
All inputs are finite; a program needn't handle non-finite values.
Results may differ from the reference program's by a relative error of at most 0.012.
Values may be sent and summed in bfloat16 or wider, within the bound.
No kernel may reach another device: no remote copies, remote signals or barrier semaphores. Data moves between devices by JAX's collectives and lax.ppermute only.
A program may use at most 32 MiB of HBM per device.

```python
import math
import jax
import jax.numpy as jnp
from jax import lax

D = 4096
HEAD_DIM = 128
TOK_DEV = 384
BAND = 256
SUMMARY = 128
HEADS = 24
TOKENS = 24576
N_CTX = 64


def draw_queries(key, part):
    base = jax.random.fold_in(key, 1)
    sample = jnp.clip(jax.random.normal(base, (TOKENS, HEADS * HEAD_DIM)), -6.0, 6.0)
    return sample.astype(jnp.float32).astype(jnp.bfloat16)


def draw_keys(key, part):
    base = jax.random.fold_in(key, 2)
    sample = jnp.clip(jax.random.normal(base, (TOKENS, HEADS * HEAD_DIM)), -6.0, 6.0)
    return sample.astype(jnp.float32).astype(jnp.bfloat16)


def shard_levels(own_key, shape, split, low, largest):
    level, own = 1.0, jax.random.fold_in(own_key, 6)
    for position, parts in split:
        heights = jnp.exp(jax.random.uniform(jax.random.fold_in(own, position), (parts,), jnp.float32, low / len(split), largest / len(split)))
        level = level * jnp.repeat(heights, shape[position] // parts).reshape([-1 if axis == position else 1 for axis in range(len(shape))])
    return level


def scatter_about(key, extent, scale, most, pieces=(), kind=jnp.bfloat16):
    array = jax.random.normal(key, extent, jnp.float32) * scale
    if len(pieces) > 0:
        array = shard_levels(key, extent, pieces, -0.22, 0.18) * array
    return jnp.clip(array, min=-most, max=most).astype(kind)


def setup_inputs(seed: int = 0) -> dict:
    arg_keys = jax.random.split(jax.random.key(seed), 5)
    queries = draw_queries(jax.random.fold_in(arg_keys[4], 71), 0)
    keys = draw_keys(jax.random.fold_in(arg_keys[4], 71), 0)
    values = scatter_about(arg_keys[2], (TOKENS, HEADS * HEAD_DIM), 1.0, 6.0, ((0, 64), (1, 12)))
    out_weight = scatter_about(arg_keys[3], (HEADS * HEAD_DIM, D), (HEADS * HEAD_DIM) ** -0.5, 0.109375, ((0, 12),))
    return dict(queries=queries, keys=keys, values=values, out_weight=out_weight)


LOW_SCORE = -1e+30

def reference(queries, keys, values, out_weight):
    scale = 1.0 / math.sqrt(HEAD_DIM)
    half_sum = SUMMARY // 2
    width = HEADS * HEAD_DIM
    sum_index = jnp.arange(N_CTX * half_sum, dtype=jnp.int32)
    sum_owner = sum_index // half_sum
    sum_pos = (sum_owner * TOK_DEV + jnp.where(sum_owner % 2 == 0, TOK_DEV - half_sum, 0) + sum_index % half_sum).astype(jnp.int32)
    sum_keys = keys[sum_pos]
    sum_values = values[sum_pos]
    pad_keys = jnp.concatenate([jnp.zeros((BAND, width), jnp.bfloat16), keys], axis=0)
    pad_values = jnp.concatenate([jnp.zeros((BAND, width), jnp.bfloat16), values], axis=0)

    def one_block(block_idx):
        first = (block_idx * TOK_DEV).astype(jnp.int32)
        query_rows = lax.dynamic_slice_in_dim(queries, first, TOK_DEV, 0)
        key_rows = lax.dynamic_slice_in_dim(pad_keys, first, TOK_DEV + BAND, 0)
        value_rows = lax.dynamic_slice_in_dim(pad_values, first, TOK_DEV + BAND, 0)
        query_pos = first + jnp.arange(TOK_DEV, dtype=jnp.int32)
        band_pos = first - BAND + jnp.arange(TOK_DEV + BAND, dtype=jnp.int32)
        band_gap = query_pos[:, None] - band_pos[None, :]
        band_mask = (band_gap >= 0) & (band_gap < BAND) & (band_pos[None, :] >= 0)
        sum_mask = query_pos[:, None] - sum_pos[None, :] >= BAND
        allowed = jnp.concatenate([band_mask, sum_mask], axis=1)
        all_keys = jnp.concatenate([key_rows, sum_keys], axis=0).astype(jnp.float32)
        all_values = jnp.concatenate([value_rows, sum_values], axis=0).astype(jnp.float32)
        q_three = query_rows.astype(jnp.float32).reshape(TOK_DEV, HEADS, HEAD_DIM)
        k_three = all_keys.reshape(-1, HEADS, HEAD_DIM)
        v_three = all_values.reshape(-1, HEADS, HEAD_DIM)
        scores = jnp.einsum('qhd,khd->hqk', q_three, k_three) * scale
        scores = jnp.where(allowed[None], scores, LOW_SCORE)
        top_score = lax.optimization_barrier(jnp.max(scores, axis=2, keepdims=True))
        weights = jnp.where(allowed[None], jnp.exp(scores - top_score), 0.0)
        totals = lax.optimization_barrier(jnp.sum(weights, axis=2))
        probs = lax.optimization_barrier(weights.astype(jnp.bfloat16)).astype(jnp.float32)
        summed = jnp.einsum('hqk,khd->qhd', probs, v_three)
        result = summed / jnp.transpose(totals)[:, :, None]
        return result.reshape(TOK_DEV, width).astype(jnp.bfloat16)
    attn = lax.map(one_block, jnp.arange(N_CTX, dtype=jnp.int32)).reshape(TOKENS, width)
    mixed = jnp.dot(attn, out_weight, preferred_element_type=jnp.float32)
    return mixed.astype(jnp.bfloat16)
```

```python
import math

import jax
import jax.numpy as jnp
from jax import lax
from jax.sharding import Mesh, PartitionSpec as P

HEAD_DIM = 128
BAND = 256
SUMMARY = 128
CTX = ("cx", "cy", "cc")
CHIPS = ("cx", "cy")
CORE = "cc"


LOW_SCORE = -1e30


def shifted(value, axis, steps):
    count = lax.axis_size(axis)
    leading, last = (max(0, -steps), min(count, count - steps))
    return lax.ppermute(value, axis, [(source, source + steps) for source in range(leading, last)])


def block_terms(query_rows, key_rows, value_rows, allowed):
    scale = 1.0 / math.sqrt(HEAD_DIM)
    head_count = query_rows.shape[1] // HEAD_DIM
    tops = []
    totals = []
    weighted = []
    for head_idx in range(head_count):
        low_col = head_idx * HEAD_DIM
        q_part = query_rows[:, low_col : low_col + HEAD_DIM]
        k_part = key_rows[:, low_col : low_col + HEAD_DIM]
        v_part = value_rows[:, low_col : low_col + HEAD_DIM]
        scores = (
            lax.dot_general(
                q_part, k_part, (((1,), (1,)), ((), ())), preferred_element_type=jnp.float32
            )
            * scale
        )
        scores = jnp.where(allowed, scores, LOW_SCORE)
        top_score = jnp.max(scores, axis=1)
        weights = jnp.where(allowed, jnp.exp(scores - top_score[:, None]), 0.0)
        tops.append(top_score)
        totals.append(jnp.sum(weights, axis=1))
        weighted.append(
            jnp.dot(weights.astype(jnp.bfloat16), v_part, preferred_element_type=jnp.float32)
        )
    return (jnp.stack(tops), jnp.stack(totals), jnp.stack(weighted))


def combine_terms(first, second):
    top_score = jnp.maximum(first[0], second[0])
    first_factor = jnp.exp(first[0] - top_score)
    second_factor = jnp.exp(second[0] - top_score)
    totals = first[1] * first_factor + second[1] * second_factor
    weighted = first[2] * first_factor[:, :, None] + second[2] * second_factor[:, :, None]
    return (top_score, totals, weighted)


def on_device(queries, keys, values, out_weight):
    tok_rows, width = queries.shape
    head_count = width // HEAD_DIM
    half_sum = SUMMARY // 2
    my_index = lax.axis_index(CTX)
    rim_keys, rim_values = shifted((keys[tok_rows - BAND :], values[tok_rows - BAND :]), CTX, 1)
    band_keys = jnp.concatenate([rim_keys, keys], axis=0)
    band_values = jnp.concatenate([rim_values, values], axis=0)
    own_pos = my_index * tok_rows + jnp.arange(tok_rows, dtype=jnp.int32)
    band_pos = my_index * tok_rows - BAND + jnp.arange(tok_rows + BAND, dtype=jnp.int32)
    band_gap = own_pos[:, None] - band_pos[None, :]
    band_mask = (band_gap >= 0) & (band_gap < BAND) & (band_pos[None, :] >= 0)
    band_part = block_terms(queries, band_keys, band_values, band_mask)
    core = lax.axis_index(CORE)
    sum_start = jnp.where(my_index % 2 == 0, tok_rows - half_sum, 0).astype(jnp.int32)
    own_keys = lax.dynamic_slice_in_dim(keys, sum_start, half_sum, 0)
    own_values = lax.dynamic_slice_in_dim(values, sum_start, half_sum, 0)
    chip_rows = lax.all_gather(
        jnp.concatenate([own_keys, own_values], axis=1), CORE, axis=0, tiled=True
    )
    my_half = lax.dynamic_slice_in_dim(chip_rows, core * width, width, 1)
    gathered = lax.all_gather(my_half, CHIPS, axis=0, tiled=True)
    both = lax.all_gather(gathered, CORE, axis=0, tiled=False)
    all_sum_keys, all_sum_values = both[0], both[1]
    sum_rows = all_sum_keys.shape[0]
    step_rows = math.gcd(sum_rows, 512)
    step_count = sum_rows // step_rows
    row_count = queries.shape[0]
    newest = jnp.max(own_pos)
    initial = (
        jnp.full((head_count, row_count), LOW_SCORE, jnp.float32),
        jnp.zeros((head_count, row_count), jnp.float32),
        jnp.zeros((head_count, row_count, HEAD_DIM), jnp.float32),
    )

    def fold_block(block_idx, carry):
        start = (block_idx * step_rows).astype(jnp.int32)
        index = start + jnp.arange(step_rows, dtype=jnp.int32)
        owner = index // half_sum
        key_pos = (
            owner * tok_rows + jnp.where(owner % 2 == 0, tok_rows - half_sum, 0) + index % half_sum
        )

        def compute(carry_in):
            key_piece = lax.dynamic_slice_in_dim(all_sum_keys, start, step_rows, 0)
            value_piece = lax.dynamic_slice_in_dim(all_sum_values, start, step_rows, 0)
            gap = own_pos[:, None] - key_pos[None, :]
            return combine_terms(
                carry_in, block_terms(queries, key_piece, value_piece, gap >= BAND)
            )

        def keep_carry(carry_in):
            return carry_in

        return lax.cond(jnp.min(key_pos) + BAND <= newest, compute, keep_carry, carry)

    far_part = lax.fori_loop(0, step_count, fold_block, initial)
    merged = combine_terms(band_part, far_part)
    heads_out = merged[2] / merged[1][:, :, None]
    attn = jnp.transpose(heads_out, (1, 0, 2)).reshape(tok_rows, width).astype(jnp.bfloat16)
    partial = jnp.dot(attn, out_weight, preferred_element_type=jnp.float32)
    return lax.psum_scatter(
        partial.astype(jnp.bfloat16), "head", scatter_dimension=0, tiled=True
    )


def solution(mesh):
    ctx_size, head_size = mesh.devices.shape
    split = mesh.devices.reshape(ctx_size // 16, 8, 2, head_size)
    fine = Mesh(split, ("cx", "cy", "cc", "head"))
    placed = (P(CTX, "head"), P(CTX, "head"), P(CTX, "head"), P("head", None))
    return jax.shard_map(
        on_device, mesh=fine, in_specs=placed, out_specs=P(CTX + ("head",), None), check_vma=False
    )
```

```python
import math

import jax
import jax.numpy as jnp
from jax import lax
from jax.sharding import Mesh, PartitionSpec as P

HEAD_DIM = 128
BAND = 256
SUMMARY = 128
CTX = ("cx", "cy", "cc")
CHIPS = ("cx", "cy")
CORE = "cc"


LOW_SCORE = -1e30


def shifted(value, axis, steps):
    count = lax.axis_size(axis)
    leading, last = (max(0, -steps), min(count, count - steps))
    return lax.ppermute(value, axis, [(source, source + steps) for source in range(leading, last)])


def block_terms(query_rows, key_rows, value_rows, allowed):
    scale = 1.0 / math.sqrt(HEAD_DIM)
    head_count = query_rows.shape[1] // HEAD_DIM
    tops = []
    totals = []
    weighted = []
    for head_idx in range(head_count):
        low_col = head_idx * HEAD_DIM
        q_part = query_rows[:, low_col : low_col + HEAD_DIM]
        k_part = key_rows[:, low_col : low_col + HEAD_DIM]
        v_part = value_rows[:, low_col : low_col + HEAD_DIM]
        scores = (
            lax.dot_general(
                q_part, k_part, (((1,), (1,)), ((), ())), preferred_element_type=jnp.float32
            )
            * scale
        )
        scores = jnp.where(allowed, scores, LOW_SCORE)
        top_score = jnp.max(scores, axis=1)
        weights = jnp.where(allowed, jnp.exp(scores - top_score[:, None]), 0.0)
        tops.append(top_score)
        totals.append(jnp.sum(weights, axis=1))
        weighted.append(
            jnp.dot(weights.astype(jnp.bfloat16), v_part, preferred_element_type=jnp.float32)
        )
    return (jnp.stack(tops), jnp.stack(totals), jnp.stack(weighted))


def combine_terms(first, second):
    top_score = jnp.maximum(first[0], second[0])
    first_factor = jnp.exp(first[0] - top_score)
    second_factor = jnp.exp(second[0] - top_score)
    totals = first[1] * first_factor + second[1] * second_factor
    weighted = first[2] * first_factor[:, :, None] + second[2] * second_factor[:, :, None]
    return (top_score, totals, weighted)


def ring_reduce_scatter(partial, axis):
    count = lax.axis_size(axis)
    me = lax.axis_index(axis)
    rows = partial.shape[0] // count
    half = partial.shape[1] // 2
    ahead = [(source, (source + 1) % count) for source in range(count)]
    behind = [(source, (source - 1) % count) for source in range(count)]

    def piece(block, low):
        start = (block % count) * rows
        return lax.dynamic_slice(partial, (start, low), (rows, half))

    up = piece(me - 1, 0).astype(jnp.bfloat16)
    down = piece(me + 1, half).astype(jnp.bfloat16)
    for step in range(count - 1):
        up_sum = lax.ppermute(up, axis, ahead).astype(jnp.float32) + piece(me - 2 - step, 0)
        down_sum = lax.ppermute(down, axis, behind).astype(jnp.float32) + piece(
            me + 2 + step, half
        )
        up = up_sum.astype(jnp.bfloat16)
        down = down_sum.astype(jnp.bfloat16)
    return jnp.concatenate([up, down], axis=1)


def on_device(queries, keys, values, out_weight):
    tok_rows, width = queries.shape
    head_count = width // HEAD_DIM
    half_sum = SUMMARY // 2
    my_index = lax.axis_index(CTX)
    rim_keys, rim_values = shifted((keys[tok_rows - BAND :], values[tok_rows - BAND :]), CTX, 1)
    band_keys = jnp.concatenate([rim_keys, keys], axis=0)
    band_values = jnp.concatenate([rim_values, values], axis=0)
    own_pos = my_index * tok_rows + jnp.arange(tok_rows, dtype=jnp.int32)
    band_pos = my_index * tok_rows - BAND + jnp.arange(tok_rows + BAND, dtype=jnp.int32)
    band_gap = own_pos[:, None] - band_pos[None, :]
    band_mask = (band_gap >= 0) & (band_gap < BAND) & (band_pos[None, :] >= 0)
    band_part = block_terms(queries, band_keys, band_values, band_mask)
    core = lax.axis_index(CORE)
    sum_start = jnp.where(my_index % 2 == 0, tok_rows - half_sum, 0).astype(jnp.int32)
    own_keys = lax.dynamic_slice_in_dim(keys, sum_start, half_sum, 0)
    own_values = lax.dynamic_slice_in_dim(values, sum_start, half_sum, 0)
    chip_rows = lax.all_gather(
        jnp.concatenate([own_keys, own_values], axis=1), CORE, axis=0, tiled=True
    )
    my_half = lax.dynamic_slice_in_dim(chip_rows, core * width, width, 1)
    gathered = lax.all_gather(my_half, "cy", axis=0, tiled=True)
    gathered = lax.all_gather(gathered, "cx", axis=0, tiled=True)
    other = lax.ppermute(gathered, CORE, [(0, 1), (1, 0)])
    both = jnp.stack([gathered, other])
    all_sum_keys = both[core]
    all_sum_values = both[1 - core]
    sum_rows = all_sum_keys.shape[0]
    step_rows = math.gcd(sum_rows, 512)
    step_count = sum_rows // step_rows
    row_count = queries.shape[0]
    newest = jnp.max(own_pos)
    initial = (
        jnp.full((head_count, row_count), LOW_SCORE, jnp.float32),
        jnp.zeros((head_count, row_count), jnp.float32),
        jnp.zeros((head_count, row_count, HEAD_DIM), jnp.float32),
    )

    def fold_block(block_idx, carry):
        start = (block_idx * step_rows).astype(jnp.int32)
        index = start + jnp.arange(step_rows, dtype=jnp.int32)
        owner = index // half_sum
        key_pos = (
            owner * tok_rows + jnp.where(owner % 2 == 0, tok_rows - half_sum, 0) + index % half_sum
        )

        def compute(carry_in):
            key_piece = lax.dynamic_slice_in_dim(all_sum_keys, start, step_rows, 0)
            value_piece = lax.dynamic_slice_in_dim(all_sum_values, start, step_rows, 0)
            gap = own_pos[:, None] - key_pos[None, :]
            return combine_terms(
                carry_in, block_terms(queries, key_piece, value_piece, gap >= BAND)
            )

        def keep_carry(carry_in):
            return carry_in

        return lax.cond(jnp.min(key_pos) + BAND <= newest, compute, keep_carry, carry)

    far_part = lax.fori_loop(0, step_count, fold_block, initial)
    merged = combine_terms(band_part, far_part)
    heads_out = merged[2] / merged[1][:, :, None]
    attn = jnp.transpose(heads_out, (1, 0, 2)).reshape(tok_rows, width).astype(jnp.bfloat16)
    partial = jnp.dot(attn, out_weight, preferred_element_type=jnp.float32)
    return ring_reduce_scatter(partial, "head")


def solution(mesh):
    ctx_size, head_size = mesh.devices.shape
    split = mesh.devices.reshape(ctx_size // 16, 8, 2, head_size)
    fine = Mesh(split, ("cx", "cy", "cc", "head"))
    placed = (P(CTX, "head"), P(CTX, "head"), P(CTX, "head"), P("head", None))
    return jax.shard_map(
        on_device, mesh=fine, in_specs=placed, out_specs=P(CTX + ("head",), None), check_vma=False
    )
```

```python
import math

import jax
import jax.numpy as jnp
from jax import lax
from jax.sharding import Mesh, PartitionSpec as P

HEAD_DIM = 128
BAND = 256
SUMMARY = 128
CTX = ("cx", "cy", "cc")
CHIPS = ("cx", "cy")
CORE = "cc"


LOW_SCORE = -1e30


def shifted(value, axis, steps):
    count = lax.axis_size(axis)
    leading, last = (max(0, -steps), min(count, count - steps))
    return lax.ppermute(value, axis, [(source, source + steps) for source in range(leading, last)])


def block_terms(query_rows, key_rows, value_rows, allowed):
    scale = 1.0 / math.sqrt(HEAD_DIM)
    head_count = query_rows.shape[1] // HEAD_DIM
    tops = []
    totals = []
    weighted = []
    for head_idx in range(head_count):
        low_col = head_idx * HEAD_DIM
        q_part = query_rows[:, low_col : low_col + HEAD_DIM]
        k_part = key_rows[:, low_col : low_col + HEAD_DIM]
        v_part = value_rows[:, low_col : low_col + HEAD_DIM]
        scores = (
            lax.dot_general(
                q_part, k_part, (((1,), (1,)), ((), ())), preferred_element_type=jnp.float32
            )
            * scale
        )
        scores = jnp.where(allowed, scores, LOW_SCORE)
        top_score = jnp.max(scores, axis=1)
        weights = jnp.where(allowed, jnp.exp(scores - top_score[:, None]), 0.0)
        tops.append(top_score)
        totals.append(jnp.sum(weights, axis=1))
        weighted.append(
            jnp.dot(weights.astype(jnp.bfloat16), v_part, preferred_element_type=jnp.float32)
        )
    return (jnp.stack(tops), jnp.stack(totals), jnp.stack(weighted))


def combine_terms(first, second):
    top_score = jnp.maximum(first[0], second[0])
    first_factor = jnp.exp(first[0] - top_score)
    second_factor = jnp.exp(second[0] - top_score)
    totals = first[1] * first_factor + second[1] * second_factor
    weighted = first[2] * first_factor[:, :, None] + second[2] * second_factor[:, :, None]
    return (top_score, totals, weighted)


def ring_reduce_scatter(partial, axis):
    count = lax.axis_size(axis)
    me = lax.axis_index(axis)
    rows = partial.shape[0] // count
    left_hops = count // 2
    right_hops = count - 1 - left_hops
    ahead = [(source, (source + 1) % count) for source in range(count)]
    behind = [(source, (source - 1) % count) for source in range(count)]

    def piece(block):
        return lax.dynamic_slice_in_dim(partial, (block % count) * rows, rows, 0)

    up = piece(me + left_hops).astype(jnp.bfloat16)
    down = piece(me - right_hops).astype(jnp.bfloat16)
    up_sum = down_sum = None
    for step in range(left_hops):
        up_sum = lax.ppermute(up, axis, ahead).astype(jnp.float32) + piece(
            me + left_hops - 1 - step
        )
        up = up_sum.astype(jnp.bfloat16)
        if step < right_hops:
            down_sum = lax.ppermute(down, axis, behind).astype(jnp.float32)
            if step < right_hops - 1:
                down_sum = down_sum + piece(me - right_hops + 1 + step)
                down = down_sum.astype(jnp.bfloat16)
    return (up_sum + down_sum).astype(jnp.bfloat16)


def on_device(queries, keys, values, out_weight):
    tok_rows, width = queries.shape
    head_count = width // HEAD_DIM
    half_sum = SUMMARY // 2
    my_index = lax.axis_index(CTX)
    rim_keys, rim_values = shifted((keys[tok_rows - BAND :], values[tok_rows - BAND :]), CTX, 1)
    band_keys = jnp.concatenate([rim_keys, keys], axis=0)
    band_values = jnp.concatenate([rim_values, values], axis=0)
    own_pos = my_index * tok_rows + jnp.arange(tok_rows, dtype=jnp.int32)
    band_pos = my_index * tok_rows - BAND + jnp.arange(tok_rows + BAND, dtype=jnp.int32)
    band_gap = own_pos[:, None] - band_pos[None, :]
    band_mask = (band_gap >= 0) & (band_gap < BAND) & (band_pos[None, :] >= 0)
    band_part = block_terms(queries, band_keys, band_values, band_mask)
    core = lax.axis_index(CORE)
    sum_start = jnp.where(my_index % 2 == 0, tok_rows - half_sum, 0).astype(jnp.int32)
    own_keys = lax.dynamic_slice_in_dim(keys, sum_start, half_sum, 0)
    own_values = lax.dynamic_slice_in_dim(values, sum_start, half_sum, 0)
    chip_rows = lax.all_gather(
        jnp.concatenate([own_keys, own_values], axis=1), CORE, axis=0, tiled=True
    )
    my_half = lax.dynamic_slice_in_dim(chip_rows, core * width, width, 1)
    gathered = lax.all_gather(my_half, "cy", axis=0, tiled=True)
    gathered = lax.all_gather(gathered, "cx", axis=0, tiled=True)
    other = lax.ppermute(gathered, CORE, [(0, 1), (1, 0)])
    both = jnp.stack([gathered, other])
    all_sum_keys = both[core]
    all_sum_values = both[1 - core]
    sum_rows = all_sum_keys.shape[0]
    step_rows = math.gcd(sum_rows, 512)
    step_count = sum_rows // step_rows
    row_count = queries.shape[0]
    newest = jnp.max(own_pos)
    initial = (
        jnp.full((head_count, row_count), LOW_SCORE, jnp.float32),
        jnp.zeros((head_count, row_count), jnp.float32),
        jnp.zeros((head_count, row_count, HEAD_DIM), jnp.float32),
    )

    def fold_block(block_idx, carry):
        start = (block_idx * step_rows).astype(jnp.int32)
        index = start + jnp.arange(step_rows, dtype=jnp.int32)
        owner = index // half_sum
        key_pos = (
            owner * tok_rows + jnp.where(owner % 2 == 0, tok_rows - half_sum, 0) + index % half_sum
        )

        def compute(carry_in):
            key_piece = lax.dynamic_slice_in_dim(all_sum_keys, start, step_rows, 0)
            value_piece = lax.dynamic_slice_in_dim(all_sum_values, start, step_rows, 0)
            gap = own_pos[:, None] - key_pos[None, :]
            return combine_terms(
                carry_in, block_terms(queries, key_piece, value_piece, gap >= BAND)
            )

        def keep_carry(carry_in):
            return carry_in

        return lax.cond(jnp.min(key_pos) + BAND <= newest, compute, keep_carry, carry)

    far_part = lax.fori_loop(0, step_count, fold_block, initial)
    merged = combine_terms(band_part, far_part)
    heads_out = merged[2] / merged[1][:, :, None]
    attn = jnp.transpose(heads_out, (1, 0, 2)).reshape(tok_rows, width).astype(jnp.bfloat16)
    partial = jnp.dot(attn, out_weight, preferred_element_type=jnp.float32)
    return ring_reduce_scatter(partial, "head")


def solution(mesh):
    ctx_size, head_size = mesh.devices.shape
    split = mesh.devices.reshape(ctx_size // 16, 8, 2, head_size)
    fine = Mesh(split, ("cx", "cy", "cc", "head"))
    placed = (P(CTX, "head"), P(CTX, "head"), P(CTX, "head"), P("head", None))
    return jax.shard_map(
        on_device, mesh=fine, in_specs=placed, out_specs=P(CTX + ("head",), None), check_vma=False
    )
```

```python
import math

import jax
import jax.numpy as jnp
from jax import lax
from jax.sharding import Mesh, PartitionSpec as P

HEAD_DIM = 128
BAND = 256
SUMMARY = 128
CTX = ("cx", "cy", "cc")
CHIPS = ("cx", "cy")
CORE = "cc"
QUERY_CHUNKS = 2


LOW_SCORE = -1e30


def shifted(value, axis, steps):
    count = lax.axis_size(axis)
    leading, last = (max(0, -steps), min(count, count - steps))
    return lax.ppermute(value, axis, [(source, source + steps) for source in range(leading, last)])


def block_terms(query_rows, key_rows, value_rows, allowed):
    scale = 1.0 / math.sqrt(HEAD_DIM)
    head_count = query_rows.shape[1] // HEAD_DIM
    tops = []
    totals = []
    weighted = []
    for head_idx in range(head_count):
        low_col = head_idx * HEAD_DIM
        q_part = query_rows[:, low_col : low_col + HEAD_DIM]
        k_part = key_rows[:, low_col : low_col + HEAD_DIM]
        v_part = value_rows[:, low_col : low_col + HEAD_DIM]
        scores = (
            lax.dot_general(
                q_part, k_part, (((1,), (1,)), ((), ())), preferred_element_type=jnp.float32
            )
            * scale
        )
        scores = jnp.where(allowed, scores, LOW_SCORE)
        top_score = jnp.max(scores, axis=1)
        weights = jnp.where(allowed, jnp.exp(scores - top_score[:, None]), 0.0)
        tops.append(top_score)
        totals.append(jnp.sum(weights, axis=1))
        weighted.append(
            jnp.dot(weights.astype(jnp.bfloat16), v_part, preferred_element_type=jnp.float32)
        )
    return (jnp.stack(tops), jnp.stack(totals), jnp.stack(weighted))


def combine_terms(first, second):
    top_score = jnp.maximum(first[0], second[0])
    first_factor = jnp.exp(first[0] - top_score)
    second_factor = jnp.exp(second[0] - top_score)
    totals = first[1] * first_factor + second[1] * second_factor
    weighted = first[2] * first_factor[:, :, None] + second[2] * second_factor[:, :, None]
    return (top_score, totals, weighted)


def attend(query_rows, *parts):
    scale = 1.0 / math.sqrt(HEAD_DIM)
    rows, width = query_rows.shape
    heads = width // HEAD_DIM
    q = query_rows.reshape(rows, heads, HEAD_DIM)
    scores = []
    for keys, _, allowed in parts:
        k = keys.reshape(keys.shape[0], heads, HEAD_DIM)
        s = jnp.einsum("qhd,khd->hqk", q, k, preferred_element_type=jnp.float32) * scale
        scores.append(jnp.where(allowed[None], s, LOW_SCORE))
    top = scores[0].max(axis=2)
    for s in scores[1:]:
        top = jnp.maximum(top, s.max(axis=2))
    total = 0.0
    summed = 0.0
    for s, (_, values, allowed) in zip(scores, parts):
        w = jnp.where(allowed[None], jnp.exp(s - top[:, :, None]), 0.0)
        total = total + w.sum(axis=2)
        v = values.reshape(values.shape[0], heads, HEAD_DIM)
        summed = summed + jnp.einsum(
            "hqk,khd->hqd", w.astype(jnp.bfloat16), v, preferred_element_type=jnp.float32
        )
    return summed / total[:, :, None]


def ring_reduce_scatter(partial, axis):
    count = lax.axis_size(axis)
    me = lax.axis_index(axis)
    rows = partial.shape[0] // count
    left_hops = count // 2
    right_hops = count - 1 - left_hops
    ahead = [(source, (source + 1) % count) for source in range(count)]
    behind = [(source, (source - 1) % count) for source in range(count)]

    def piece(block):
        return lax.dynamic_slice_in_dim(partial, (block % count) * rows, rows, 0)

    up = piece(me + left_hops).astype(jnp.bfloat16)
    down = piece(me - right_hops).astype(jnp.bfloat16)
    up_sum = down_sum = None
    for step in range(left_hops):
        up_sum = lax.ppermute(up, axis, ahead).astype(jnp.float32) + piece(
            me + left_hops - 1 - step
        )
        up = up_sum.astype(jnp.bfloat16)
        if step < right_hops:
            down_sum = lax.ppermute(down, axis, behind).astype(jnp.float32)
            if step < right_hops - 1:
                down_sum = down_sum + piece(me - right_hops + 1 + step)
                down = down_sum.astype(jnp.bfloat16)
    return (up_sum + down_sum).astype(jnp.bfloat16)


def on_device(queries, keys, values, out_weight):
    tok_rows, width = queries.shape
    head_count = width // HEAD_DIM
    half_sum = SUMMARY // 2
    my_index = lax.axis_index(CTX)
    rim_keys, rim_values = shifted((keys[tok_rows - BAND :], values[tok_rows - BAND :]), CTX, 1)
    band_keys = jnp.concatenate([rim_keys, keys], axis=0)
    band_values = jnp.concatenate([rim_values, values], axis=0)
    own_pos = my_index * tok_rows + jnp.arange(tok_rows, dtype=jnp.int32)
    band_pos = my_index * tok_rows - BAND + jnp.arange(tok_rows + BAND, dtype=jnp.int32)
    band_gap = own_pos[:, None] - band_pos[None, :]
    band_mask = (band_gap >= 0) & (band_gap < BAND) & (band_pos[None, :] >= 0)
    core = lax.axis_index(CORE)
    sum_start = jnp.where(my_index % 2 == 0, tok_rows - half_sum, 0).astype(jnp.int32)
    own_keys = lax.dynamic_slice_in_dim(keys, sum_start, half_sum, 0)
    own_values = lax.dynamic_slice_in_dim(values, sum_start, half_sum, 0)
    chip_rows = lax.all_gather(
        jnp.concatenate([own_keys, own_values], axis=1), CORE, axis=0, tiled=True
    )
    my_half = lax.dynamic_slice_in_dim(chip_rows, core * width, width, 1)
    gathered = lax.all_gather(my_half, "cy", axis=0, tiled=True)
    gathered = lax.all_gather(gathered, "cx", axis=0, tiled=True)
    other = lax.ppermute(gathered, CORE, [(0, 1), (1, 0)])
    both = jnp.stack([gathered, other])
    all_sum_keys = both[core]
    all_sum_values = both[1 - core]
    index = jnp.arange(all_sum_keys.shape[0], dtype=jnp.int32)
    owner = index // half_sum
    key_pos = owner * tok_rows + jnp.where(owner % 2 == 0, tok_rows - half_sum, 0) + index % half_sum
    sum_mask = own_pos[:, None] - key_pos[None, :] >= BAND
    pieces = []
    chunk = tok_rows // QUERY_CHUNKS
    for low in range(0, tok_rows, chunk):
        pieces.append(
            attend(
                queries[low : low + chunk],
                (band_keys, band_values, band_mask[low : low + chunk]),
                (all_sum_keys, all_sum_values, sum_mask[low : low + chunk]),
            )
        )
    heads_out = jnp.concatenate(pieces, axis=1)
    attn = jnp.transpose(heads_out, (1, 0, 2)).reshape(tok_rows, width).astype(jnp.bfloat16)
    partial = jnp.dot(attn, out_weight, preferred_element_type=jnp.float32)
    return ring_reduce_scatter(partial, "head")


def solution(mesh):
    ctx_size, head_size = mesh.devices.shape
    split = mesh.devices.reshape(ctx_size // 16, 8, 2, head_size)
    fine = Mesh(split, ("cx", "cy", "cc", "head"))
    placed = (P(CTX, "head"), P(CTX, "head"), P(CTX, "head"), P("head", None))
    return jax.shard_map(
        on_device, mesh=fine, in_specs=placed, out_specs=P(CTX + ("head",), None), check_vma=False
    )
```

```python
import math

import jax
import jax.numpy as jnp
from jax import lax
from jax.sharding import Mesh, PartitionSpec as P

HEAD_DIM = 128
BAND = 256
SUMMARY = 128
CTX = ("cx", "cy", "cc")
CORE = "cc"
QUERY_CHUNKS = 2


LOW_SCORE = -1e30


def shifted(value, axis, steps):
    count = lax.axis_size(axis)
    leading, last = (max(0, -steps), min(count, count - steps))
    return lax.ppermute(value, axis, [(source, source + steps) for source in range(leading, last)])


def combine_terms(first, second):
    top_score = jnp.maximum(first[0], second[0])
    first_factor = jnp.exp(first[0] - top_score)
    second_factor = jnp.exp(second[0] - top_score)
    totals = first[1] * first_factor + second[1] * second_factor
    weighted = first[2] * first_factor[:, :, None] + second[2] * second_factor[:, :, None]
    return (top_score, totals, weighted)


def attend(query_rows, keys, values, allowed):
    scale = 1.0 / math.sqrt(HEAD_DIM)
    rows, width = query_rows.shape
    heads = width // HEAD_DIM
    q = query_rows.reshape(rows, heads, HEAD_DIM)
    k = keys.reshape(keys.shape[0], heads, HEAD_DIM)
    s = jnp.einsum("qhd,khd->hqk", q, k, preferred_element_type=jnp.float32) * scale
    s = jnp.where(allowed[None], s, LOW_SCORE)
    top = s.max(axis=2)
    w = jnp.where(allowed[None], jnp.exp(s - top[:, :, None]), 0.0)
    v = values.reshape(values.shape[0], heads, HEAD_DIM)
    summed = jnp.einsum(
        "hqk,khd->hqd", w.astype(jnp.bfloat16), v, preferred_element_type=jnp.float32
    )
    return top, w.sum(axis=2), summed


def ring_reduce_scatter(partial, axis):
    count = lax.axis_size(axis)
    me = lax.axis_index(axis)
    rows = partial.shape[0] // count
    left_hops = count // 2
    right_hops = count - 1 - left_hops
    ahead = [(source, (source + 1) % count) for source in range(count)]
    behind = [(source, (source - 1) % count) for source in range(count)]

    def piece(block):
        return lax.dynamic_slice_in_dim(partial, (block % count) * rows, rows, 0)

    up = piece(me + left_hops).astype(jnp.bfloat16)
    down = piece(me - right_hops).astype(jnp.bfloat16)
    up_sum = down_sum = None
    for step in range(left_hops):
        up_sum = lax.ppermute(up, axis, ahead).astype(jnp.float32) + piece(
            me + left_hops - 1 - step
        )
        up = up_sum.astype(jnp.bfloat16)
        if step < right_hops:
            down_sum = lax.ppermute(down, axis, behind).astype(jnp.float32)
            if step < right_hops - 1:
                down_sum = down_sum + piece(me - right_hops + 1 + step)
                down = down_sum.astype(jnp.bfloat16)
    return (up_sum + down_sum).astype(jnp.bfloat16)


def layer(queries, keys, values, out_weight):
    tok_rows, width = queries.shape
    half_sum = SUMMARY // 2
    my_index = lax.axis_index(CTX)
    rim_keys, rim_values = shifted((keys[tok_rows - BAND :], values[tok_rows - BAND :]), CTX, 1)
    band_keys = jnp.concatenate([rim_keys, keys], axis=0)
    band_values = jnp.concatenate([rim_values, values], axis=0)
    own_pos = my_index * tok_rows + jnp.arange(tok_rows, dtype=jnp.int32)
    band_pos = my_index * tok_rows - BAND + jnp.arange(tok_rows + BAND, dtype=jnp.int32)
    band_gap = own_pos[:, None] - band_pos[None, :]
    band_mask = (band_gap >= 0) & (band_gap < BAND) & (band_pos[None, :] >= 0)
    chunk = tok_rows // QUERY_CHUNKS
    near = [
        attend(queries[low : low + chunk], band_keys, band_values, band_mask[low : low + chunk])
        for low in range(0, tok_rows, chunk)
    ]
    core = lax.axis_index(CORE)
    sum_start = jnp.where(my_index % 2 == 0, tok_rows - half_sum, 0).astype(jnp.int32)
    own_keys = lax.dynamic_slice_in_dim(keys, sum_start, half_sum, 0)
    own_values = lax.dynamic_slice_in_dim(values, sum_start, half_sum, 0)
    chip_rows = lax.all_gather(
        jnp.concatenate([own_keys, own_values], axis=1), CORE, axis=0, tiled=True
    )
    my_half = lax.dynamic_slice_in_dim(chip_rows, core * width, width, 1)
    ring = lax.axis_size("cy")
    gathered = my_half
    shift = 1
    while shift < ring:
        moved = lax.ppermute(gathered, "cy", [(j, (j + shift) % ring) for j in range(ring)])
        gathered = jnp.concatenate([gathered, moved], axis=0)
        shift *= 2
    gathered = lax.all_gather(gathered, "cx", axis=0, tiled=True)
    other = lax.ppermute(gathered, CORE, [(0, 1), (1, 0)])
    both = jnp.stack([gathered, other])
    all_sum_keys = both[core]
    all_sum_values = both[1 - core]
    index = jnp.arange(all_sum_keys.shape[0], dtype=jnp.int32)
    across = index // (SUMMARY * ring)
    back = (index // SUMMARY) % ring
    chip = across * ring + (lax.axis_index("cy") - back) % ring
    key_pos = chip * 2 * tok_rows + tok_rows - half_sum + index % SUMMARY
    sum_mask = own_pos[:, None] - key_pos[None, :] >= BAND
    pieces = []
    for low in range(0, tok_rows, chunk):
        rows = slice(low, low + chunk)
        far = attend(queries[rows], all_sum_keys, all_sum_values, sum_mask[rows])
        merged = combine_terms(near[low // chunk], far)
        pieces.append(merged[2] / merged[1][:, :, None])
    heads_out = jnp.concatenate(pieces, axis=1)
    attn = jnp.transpose(heads_out, (1, 0, 2)).reshape(tok_rows, width).astype(jnp.bfloat16)
    partial = jnp.dot(attn, out_weight, preferred_element_type=jnp.float32)
    return ring_reduce_scatter(partial, "head")


def solution(mesh):
    ctx_size, head_size = mesh.devices.shape
    split = mesh.devices.reshape(ctx_size // 16, 8, 2, head_size)
    fine = Mesh(split, ("cx", "cy", "cc", "head"))
    placed = (P(CTX, "head"), P(CTX, "head"), P(CTX, "head"), P("head", None))
    return jax.shard_map(
        layer, mesh=fine, in_specs=placed, out_specs=P(CTX + ("head",), None), check_vma=False
    )
```

```python
import math

import jax
import jax.numpy as jnp
from jax import lax
from jax.sharding import Mesh, PartitionSpec as P

HEAD_DIM = 128
BAND = 256
SUMMARY = 128
CTX = ("cx", "cy", "cc")
CORE = "cc"
QUERY_CHUNKS = 2


LOW_SCORE = -1e30


def shifted(value, axis, steps):
    count = lax.axis_size(axis)
    leading, last = (max(0, -steps), min(count, count - steps))
    return lax.ppermute(value, axis, [(source, source + steps) for source in range(leading, last)])


def combine_terms(first, second):
    top_score = jnp.maximum(first[0], second[0])
    first_factor = jnp.exp(first[0] - top_score)
    second_factor = jnp.exp(second[0] - top_score)
    totals = first[1] * first_factor + second[1] * second_factor
    weighted = first[2] * first_factor[:, :, None] + second[2] * second_factor[:, :, None]
    return (top_score, totals, weighted)


def attend(query_rows, keys, values, allowed):
    scale = 1.0 / math.sqrt(HEAD_DIM)
    rows, width = query_rows.shape
    heads = width // HEAD_DIM
    q = query_rows.reshape(rows, heads, HEAD_DIM)
    k = keys.reshape(keys.shape[0], heads, HEAD_DIM)
    s = jnp.einsum("qhd,khd->hqk", q, k, preferred_element_type=jnp.float32) * scale
    s = jnp.where(allowed[None], s, LOW_SCORE)
    top = s.max(axis=2)
    w = jnp.where(allowed[None], jnp.exp(s - top[:, :, None]), 0.0)
    v = values.reshape(values.shape[0], heads, HEAD_DIM)
    summed = jnp.einsum(
        "hqk,khd->hqd", w.astype(jnp.bfloat16), v, preferred_element_type=jnp.float32
    )
    return top, w.sum(axis=2), summed


def ring_reduce_scatter(partial, axis):
    count = lax.axis_size(axis)
    me = lax.axis_index(axis)
    rows = partial.shape[0] // count
    left_hops = count // 2
    right_hops = count - 1 - left_hops
    ahead = [(source, (source + 1) % count) for source in range(count)]
    behind = [(source, (source - 1) % count) for source in range(count)]

    def piece(block):
        return lax.dynamic_slice_in_dim(partial, (block % count) * rows, rows, 0)

    up = piece(me + left_hops).astype(jnp.bfloat16)
    down = piece(me - right_hops).astype(jnp.bfloat16)
    up_sum = down_sum = None
    for step in range(left_hops):
        up_sum = lax.ppermute(up, axis, ahead).astype(jnp.float32) + piece(
            me + left_hops - 1 - step
        )
        up = up_sum.astype(jnp.bfloat16)
        if step < right_hops:
            down_sum = lax.ppermute(down, axis, behind).astype(jnp.float32)
            if step < right_hops - 1:
                down_sum = down_sum + piece(me - right_hops + 1 + step)
                down = down_sum.astype(jnp.bfloat16)
    return (up_sum + down_sum).astype(jnp.bfloat16)


def layer(queries, keys, values, out_weight):
    tok_rows, width = queries.shape
    half_sum = SUMMARY // 2
    my_index = lax.axis_index(CTX)
    rim_keys, rim_values = shifted((keys[tok_rows - BAND :], values[tok_rows - BAND :]), CTX, 1)
    band_keys = jnp.concatenate([rim_keys, keys], axis=0)
    band_values = jnp.concatenate([rim_values, values], axis=0)
    own_pos = my_index * tok_rows + jnp.arange(tok_rows, dtype=jnp.int32)
    band_pos = my_index * tok_rows - BAND + jnp.arange(tok_rows + BAND, dtype=jnp.int32)
    band_gap = own_pos[:, None] - band_pos[None, :]
    band_mask = (band_gap >= 0) & (band_gap < BAND) & (band_pos[None, :] >= 0)
    chunk = tok_rows // QUERY_CHUNKS
    near = [
        attend(queries[low : low + chunk], band_keys, band_values, band_mask[low : low + chunk])
        for low in range(0, tok_rows, chunk)
    ]
    core = lax.axis_index(CORE)
    sum_start = jnp.where(my_index % 2 == 0, tok_rows - half_sum, 0).astype(jnp.int32)
    own_keys = lax.dynamic_slice_in_dim(keys, sum_start, half_sum, 0)
    own_values = lax.dynamic_slice_in_dim(values, sum_start, half_sum, 0)
    chip_rows = lax.all_gather(
        jnp.concatenate([own_keys, own_values], axis=1), CORE, axis=0, tiled=True
    )
    my_half = lax.dynamic_slice_in_dim(chip_rows, core * width, width, 1)
    gathered = lax.all_gather(my_half, "cy", axis=0, tiled=True)
    gathered = lax.all_gather(gathered, "cx", axis=0, tiled=True)
    other = lax.ppermute(gathered, CORE, [(0, 1), (1, 0)])
    both = jnp.stack([gathered, other])
    all_sum_keys = both[core]
    all_sum_values = both[1 - core]
    index = jnp.arange(all_sum_keys.shape[0], dtype=jnp.int32)
    owner = index // half_sum
    key_pos = owner * tok_rows + jnp.where(owner % 2 == 0, tok_rows - half_sum, 0) + index % half_sum
    sum_mask = own_pos[:, None] - key_pos[None, :] >= BAND
    pieces = []
    for low in range(0, tok_rows, chunk):
        rows = slice(low, low + chunk)
        far = attend(queries[rows], all_sum_keys, all_sum_values, sum_mask[rows])
        merged = combine_terms(near[low // chunk], far)
        pieces.append(merged[2] / merged[1][:, :, None])
    heads_out = jnp.concatenate(pieces, axis=1)
    attn = jnp.transpose(heads_out, (1, 0, 2)).reshape(tok_rows, width).astype(jnp.bfloat16)
    partial = jnp.dot(attn, out_weight, preferred_element_type=jnp.float32)
    return ring_reduce_scatter(partial, "head")


def solution(mesh):
    ctx_size, head_size = mesh.devices.shape
    split = mesh.devices.reshape(ctx_size // 16, 8, 2, head_size)
    fine = Mesh(split, ("cx", "cy", "cc", "head"))
    placed = (P(CTX, "head"), P(CTX, "head"), P(CTX, "head"), P("head", None))
    return jax.shard_map(
        layer, mesh=fine, in_specs=placed, out_specs=P(CTX + ("head",), None), check_vma=False
    )
```

```python
import math

import jax
import jax.numpy as jnp
from jax import lax
from jax.sharding import Mesh, PartitionSpec as P

HEAD_DIM = 128
BAND = 256
SUMMARY = 128
CTX = ("cx", "cy", "cc")
CORE = "cc"
QUERY_CHUNKS = 2


LOW_SCORE = -1e30


def shifted(value, axis, steps):
    count = lax.axis_size(axis)
    leading, last = (max(0, -steps), min(count, count - steps))
    return lax.ppermute(value, axis, [(source, source + steps) for source in range(leading, last)])


def combine_terms(first, second):
    top_score = jnp.maximum(first[0], second[0])
    first_factor = jnp.exp(first[0] - top_score)
    second_factor = jnp.exp(second[0] - top_score)
    totals = first[1] * first_factor + second[1] * second_factor
    weighted = first[2] * first_factor[:, :, None] + second[2] * second_factor[:, :, None]
    return (top_score, totals, weighted)


def attend(query_rows, keys, values, allowed):
    scale = 1.0 / math.sqrt(HEAD_DIM)
    rows, width = query_rows.shape
    heads = width // HEAD_DIM
    q = query_rows.reshape(rows, heads, HEAD_DIM)
    k = keys.reshape(keys.shape[0], heads, HEAD_DIM)
    s = jnp.einsum("qhd,khd->hqk", q, k, preferred_element_type=jnp.float32) * scale
    s = jnp.where(allowed[None], s, LOW_SCORE)
    top = s.max(axis=2)
    w = jnp.where(allowed[None], jnp.exp(s - top[:, :, None]), 0.0)
    v = values.reshape(values.shape[0], heads, HEAD_DIM)
    summed = jnp.einsum(
        "hqk,khd->hqd", w.astype(jnp.bfloat16), v, preferred_element_type=jnp.float32
    )
    return top, w.sum(axis=2), summed


def gather_row_blocks(block, axis):
    count = lax.axis_size(axis)
    if count != 4:
        gathered = lax.all_gather(block, axis, axis=0, tiled=True)
        me = lax.axis_index(axis)
        return gathered, [(j - me) for j in range(count)]
    ahead = [(j, (j + 1) % count) for j in range(count)]
    behind = [(j, (j - 1) % count) for j in range(count)]
    from_left = lax.ppermute(block, axis, ahead)
    from_right = lax.ppermute(block, axis, behind)
    half = block.shape[0] // 2
    far = jnp.concatenate(
        [
            lax.ppermute(from_left[:half], axis, ahead),
            lax.ppermute(from_right[half:], axis, behind),
        ],
        axis=0,
    )
    return jnp.concatenate([block, from_left, far, from_right], axis=0), [0, -1, -2, 1]


def ring_reduce_scatter(partial, axis):
    count = lax.axis_size(axis)
    me = lax.axis_index(axis)
    rows = partial.shape[0] // count
    left_hops = count // 2
    right_hops = count - 1 - left_hops
    ahead = [(source, (source + 1) % count) for source in range(count)]
    behind = [(source, (source - 1) % count) for source in range(count)]

    def piece(block):
        return lax.dynamic_slice_in_dim(partial, (block % count) * rows, rows, 0)

    up = piece(me + left_hops).astype(jnp.bfloat16)
    down = piece(me - right_hops).astype(jnp.bfloat16)
    up_sum = down_sum = None
    for step in range(left_hops):
        up_sum = lax.ppermute(up, axis, ahead).astype(jnp.float32) + piece(
            me + left_hops - 1 - step
        )
        up = up_sum.astype(jnp.bfloat16)
        if step < right_hops:
            down_sum = lax.ppermute(down, axis, behind).astype(jnp.float32)
            if step < right_hops - 1:
                down_sum = down_sum + piece(me - right_hops + 1 + step)
                down = down_sum.astype(jnp.bfloat16)
    return (up_sum + down_sum).astype(jnp.bfloat16)


def layer(queries, keys, values, out_weight):
    tok_rows, width = queries.shape
    half_sum = SUMMARY // 2
    my_index = lax.axis_index(CTX)
    rim_keys, rim_values = shifted((keys[tok_rows - BAND :], values[tok_rows - BAND :]), CTX, 1)
    band_keys = jnp.concatenate([rim_keys, keys], axis=0)
    band_values = jnp.concatenate([rim_values, values], axis=0)
    own_pos = my_index * tok_rows + jnp.arange(tok_rows, dtype=jnp.int32)
    band_pos = my_index * tok_rows - BAND + jnp.arange(tok_rows + BAND, dtype=jnp.int32)
    band_gap = own_pos[:, None] - band_pos[None, :]
    band_mask = (band_gap >= 0) & (band_gap < BAND) & (band_pos[None, :] >= 0)
    chunk = tok_rows // QUERY_CHUNKS
    near = [
        attend(queries[low : low + chunk], band_keys, band_values, band_mask[low : low + chunk])
        for low in range(0, tok_rows, chunk)
    ]
    core = lax.axis_index(CORE)
    sum_start = jnp.where(my_index % 2 == 0, tok_rows - half_sum, 0).astype(jnp.int32)
    own_keys = lax.dynamic_slice_in_dim(keys, sum_start, half_sum, 0)
    own_values = lax.dynamic_slice_in_dim(values, sum_start, half_sum, 0)
    chip_rows = lax.all_gather(
        jnp.concatenate([own_keys, own_values], axis=1), CORE, axis=0, tiled=True
    )
    my_half = lax.dynamic_slice_in_dim(chip_rows, core * width, width, 1)
    gathered = lax.all_gather(my_half, "cy", axis=0, tiled=True)
    gathered, offsets = gather_row_blocks(gathered, "cx")
    other = lax.ppermute(gathered, CORE, [(0, 1), (1, 0)])
    both = jnp.stack([gathered, other])
    all_sum_keys = both[core]
    all_sum_values = both[1 - core]
    index = jnp.arange(all_sum_keys.shape[0], dtype=jnp.int32)
    row_len = index.shape[0] // len(offsets)
    x_count = lax.axis_size("cx")
    moved = jnp.asarray(offsets, jnp.int32)[index // row_len]
    source_x = (lax.axis_index("cx") + moved) % x_count
    owner = source_x * (row_len // half_sum) + (index % row_len) // half_sum
    key_pos = owner * tok_rows + jnp.where(owner % 2 == 0, tok_rows - half_sum, 0) + index % half_sum
    sum_mask = own_pos[:, None] - key_pos[None, :] >= BAND
    pieces = []
    for low in range(0, tok_rows, chunk):
        rows = slice(low, low + chunk)
        far = attend(queries[rows], all_sum_keys, all_sum_values, sum_mask[rows])
        merged = combine_terms(near[low // chunk], far)
        pieces.append(merged[2] / merged[1][:, :, None])
    heads_out = jnp.concatenate(pieces, axis=1)
    attn = jnp.transpose(heads_out, (1, 0, 2)).reshape(tok_rows, width).astype(jnp.bfloat16)
    partial = jnp.dot(attn, out_weight, preferred_element_type=jnp.float32)
    return ring_reduce_scatter(partial, "head")


def solution(mesh):
    ctx_size, head_size = mesh.devices.shape
    split = mesh.devices.reshape(ctx_size // 16, 8, 2, head_size)
    fine = Mesh(split, ("cx", "cy", "cc", "head"))
    placed = (P(CTX, "head"), P(CTX, "head"), P(CTX, "head"), P("head", None))
    return jax.shard_map(
        layer, mesh=fine, in_specs=placed, out_specs=P(CTX + ("head",), None), check_vma=False
    )
```

```python
import math

import jax
import jax.numpy as jnp
from jax import lax
from jax.sharding import Mesh, PartitionSpec as P

HEAD_DIM = 128
BAND = 256
SUMMARY = 128
CTX = ("cx", "cy", "cc")
CORE = "cc"
QUERY_CHUNKS = 2


LOW_SCORE = -1e30


def shifted(value, axis, steps):
    count = lax.axis_size(axis)
    leading, last = (max(0, -steps), min(count, count - steps))
    return lax.ppermute(value, axis, [(source, source + steps) for source in range(leading, last)])


def combine_terms(first, second):
    top_score = jnp.maximum(first[0], second[0])
    first_factor = jnp.exp(first[0] - top_score)
    second_factor = jnp.exp(second[0] - top_score)
    totals = first[1] * first_factor + second[1] * second_factor
    weighted = first[2] * first_factor[:, :, None] + second[2] * second_factor[:, :, None]
    return (top_score, totals, weighted)


def attend(query_rows, parts):
    scale = 1.0 / math.sqrt(HEAD_DIM)
    rows, width = query_rows.shape
    heads = width // HEAD_DIM
    q = query_rows.reshape(rows, heads, HEAD_DIM)
    scores = []
    for keys, _, allowed in parts:
        k = keys.reshape(keys.shape[0], heads, HEAD_DIM)
        s = jnp.einsum("qhd,khd->hqk", q, k, preferred_element_type=jnp.float32) * scale
        scores.append(jnp.where(allowed[None], s, LOW_SCORE))
    top = scores[0].max(axis=2)
    for s in scores[1:]:
        top = jnp.maximum(top, s.max(axis=2))
    total = 0.0
    summed = 0.0
    for s, (_, values, allowed) in zip(scores, parts):
        w = jnp.where(allowed[None], jnp.exp(s - top[:, :, None]), 0.0)
        total = total + w.sum(axis=2)
        v = values.reshape(values.shape[0], heads, HEAD_DIM)
        summed = summed + jnp.einsum(
            "hqk,khd->hqd", w.astype(jnp.bfloat16), v, preferred_element_type=jnp.float32
        )
    return top, total, summed


def gather_row_blocks(block, axis):
    count = lax.axis_size(axis)
    if count != 4:
        gathered = lax.all_gather(block, axis, axis=0, tiled=True)
        me = lax.axis_index(axis)
        rows = block.shape[0]
        return [gathered[j * rows : (j + 1) * rows] for j in range(count)], [
            j - me for j in range(count)
        ]
    ahead = [(j, (j + 1) % count) for j in range(count)]
    behind = [(j, (j - 1) % count) for j in range(count)]
    from_left = lax.ppermute(block, axis, ahead)
    from_right = lax.ppermute(block, axis, behind)
    half = block.shape[0] // 2
    far = jnp.concatenate(
        [
            lax.ppermute(from_left[:half], axis, ahead),
            lax.ppermute(from_right[half:], axis, behind),
        ],
        axis=0,
    )
    return [block, from_left, far, from_right], [0, -1, -2, 1]


def ring_reduce_scatter(partial, axis):
    count = lax.axis_size(axis)
    me = lax.axis_index(axis)
    rows = partial.shape[0] // count
    left_hops = count // 2
    right_hops = count - 1 - left_hops
    ahead = [(source, (source + 1) % count) for source in range(count)]
    behind = [(source, (source - 1) % count) for source in range(count)]

    def piece(block):
        return lax.dynamic_slice_in_dim(partial, (block % count) * rows, rows, 0)

    up = piece(me + left_hops).astype(jnp.bfloat16)
    down = piece(me - right_hops).astype(jnp.bfloat16)
    up_sum = down_sum = None
    for step in range(left_hops):
        up_sum = lax.ppermute(up, axis, ahead).astype(jnp.float32) + piece(
            me + left_hops - 1 - step
        )
        up = up_sum.astype(jnp.bfloat16)
        if step < right_hops:
            down_sum = lax.ppermute(down, axis, behind).astype(jnp.float32)
            if step < right_hops - 1:
                down_sum = down_sum + piece(me - right_hops + 1 + step)
                down = down_sum.astype(jnp.bfloat16)
    return (up_sum + down_sum).astype(jnp.bfloat16)


def layer(queries, keys, values, out_weight):
    tok_rows, width = queries.shape
    half_sum = SUMMARY // 2
    my_index = lax.axis_index(CTX)
    rim_keys, rim_values = shifted((keys[tok_rows - BAND :], values[tok_rows - BAND :]), CTX, 1)
    band_keys = jnp.concatenate([rim_keys, keys], axis=0)
    band_values = jnp.concatenate([rim_values, values], axis=0)
    own_pos = my_index * tok_rows + jnp.arange(tok_rows, dtype=jnp.int32)
    band_pos = my_index * tok_rows - BAND + jnp.arange(tok_rows + BAND, dtype=jnp.int32)
    band_gap = own_pos[:, None] - band_pos[None, :]
    band_mask = (band_gap >= 0) & (band_gap < BAND) & (band_pos[None, :] >= 0)
    chunk = tok_rows // QUERY_CHUNKS
    near = [
        attend(queries[low : low + chunk], [(band_keys, band_values, band_mask[low : low + chunk])])
        for low in range(0, tok_rows, chunk)
    ]
    core = lax.axis_index(CORE)
    sum_start = jnp.where(my_index % 2 == 0, tok_rows - half_sum, 0).astype(jnp.int32)
    own_keys = lax.dynamic_slice_in_dim(keys, sum_start, half_sum, 0)
    own_values = lax.dynamic_slice_in_dim(values, sum_start, half_sum, 0)
    chip_rows = lax.all_gather(
        jnp.concatenate([own_keys, own_values], axis=1), CORE, axis=0, tiled=True
    )
    my_half = lax.dynamic_slice_in_dim(chip_rows, core * width, width, 1)
    gathered = lax.all_gather(my_half, "cy", axis=0, tiled=True)
    blocks, offsets = gather_row_blocks(gathered, "cx")
    others = lax.ppermute(tuple(blocks), CORE, [(0, 1), (1, 0)])
    first = core == 0
    row_len = blocks[0].shape[0]
    index = jnp.arange(row_len, dtype=jnp.int32)
    far_parts = []
    for mine, other, moved in zip(blocks, others, offsets):
        source_x = (lax.axis_index("cx") + moved) % lax.axis_size("cx")
        owner = source_x * (row_len // half_sum) + index // half_sum
        key_pos = owner * tok_rows + jnp.where(owner % 2 == 0, tok_rows - half_sum, 0) + index % half_sum
        allowed = own_pos[:, None] - key_pos[None, :] >= BAND
        far_parts.append((jnp.where(first, mine, other), jnp.where(first, other, mine), allowed))
    pieces = []
    for low in range(0, tok_rows, chunk):
        rows = slice(low, low + chunk)
        far = attend(queries[rows], [(k, v, ok[rows]) for k, v, ok in far_parts])
        merged = combine_terms(near[low // chunk], far)
        pieces.append(merged[2] / merged[1][:, :, None])
    heads_out = jnp.concatenate(pieces, axis=1)
    attn = jnp.transpose(heads_out, (1, 0, 2)).reshape(tok_rows, width).astype(jnp.bfloat16)
    partial = jnp.dot(attn, out_weight, preferred_element_type=jnp.float32)
    return ring_reduce_scatter(partial, "head")


def solution(mesh):
    ctx_size, head_size = mesh.devices.shape
    split = mesh.devices.reshape(ctx_size // 16, 8, 2, head_size)
    fine = Mesh(split, ("cx", "cy", "cc", "head"))
    placed = (P(CTX, "head"), P(CTX, "head"), P(CTX, "head"), P("head", None))
    return jax.shard_map(
        layer, mesh=fine, in_specs=placed, out_specs=P(CTX + ("head",), None), check_vma=False
    )
```

```python
import math

import jax
import jax.numpy as jnp
from jax import lax
from jax.sharding import Mesh, PartitionSpec as P

HEAD_DIM = 128
BAND = 256
SUMMARY = 128
CTX = ("cx", "cy", "cc")
CORE = "cc"
QUERY_CHUNKS = 1


LOW_SCORE = -1e30


def shifted(value, axis, steps):
    count = lax.axis_size(axis)
    leading, last = (max(0, -steps), min(count, count - steps))
    return lax.ppermute(value, axis, [(source, source + steps) for source in range(leading, last)])


def combine_terms(first, second):
    top_score = jnp.maximum(first[0], second[0])
    first_factor = jnp.exp(first[0] - top_score)
    second_factor = jnp.exp(second[0] - top_score)
    totals = first[1] * first_factor + second[1] * second_factor
    weighted = first[2] * first_factor[:, :, None] + second[2] * second_factor[:, :, None]
    return (top_score, totals, weighted)


def attend(query_rows, keys, values, allowed):
    scale = 1.0 / math.sqrt(HEAD_DIM)
    rows, width = query_rows.shape
    heads = width // HEAD_DIM
    q = query_rows.reshape(rows, heads, HEAD_DIM)
    k = keys.reshape(keys.shape[0], heads, HEAD_DIM)
    s = jnp.einsum("qhd,khd->hqk", q, k, preferred_element_type=jnp.float32) * scale
    s = jnp.where(allowed[None], s, LOW_SCORE)
    top = s.max(axis=2)
    w = jnp.where(allowed[None], jnp.exp(s - top[:, :, None]), 0.0)
    v = values.reshape(values.shape[0], heads, HEAD_DIM)
    summed = jnp.einsum(
        "hqk,khd->hqd", w.astype(jnp.bfloat16), v, preferred_element_type=jnp.float32
    )
    return top, w.sum(axis=2), summed


def gather_row_blocks(block, axis):
    count = lax.axis_size(axis)
    if count != 4:
        gathered = lax.all_gather(block, axis, axis=0, tiled=True)
        me = lax.axis_index(axis)
        return gathered, [(j - me) for j in range(count)]
    ahead = [(j, (j + 1) % count) for j in range(count)]
    behind = [(j, (j - 1) % count) for j in range(count)]
    from_left = lax.ppermute(block, axis, ahead)
    from_right = lax.ppermute(block, axis, behind)
    half = block.shape[0] // 2
    far = jnp.concatenate(
        [
            lax.ppermute(from_left[:half], axis, ahead),
            lax.ppermute(from_right[half:], axis, behind),
        ],
        axis=0,
    )
    return jnp.concatenate([block, from_left, far, from_right], axis=0), [0, -1, -2, 1]


def ring_reduce_scatter(partial, axis):
    count = lax.axis_size(axis)
    me = lax.axis_index(axis)
    rows = partial.shape[0] // count
    left_hops = count // 2
    right_hops = count - 1 - left_hops
    ahead = [(source, (source + 1) % count) for source in range(count)]
    behind = [(source, (source - 1) % count) for source in range(count)]

    def piece(block):
        return lax.dynamic_slice_in_dim(partial, (block % count) * rows, rows, 0)

    up = piece(me + left_hops).astype(jnp.bfloat16)
    down = piece(me - right_hops).astype(jnp.bfloat16)
    up_sum = down_sum = None
    for step in range(left_hops):
        up_sum = lax.ppermute(up, axis, ahead).astype(jnp.float32) + piece(
            me + left_hops - 1 - step
        )
        up = up_sum.astype(jnp.bfloat16)
        if step < right_hops:
            down_sum = lax.ppermute(down, axis, behind).astype(jnp.float32)
            if step < right_hops - 1:
                down_sum = down_sum + piece(me - right_hops + 1 + step)
                down = down_sum.astype(jnp.bfloat16)
    return (up_sum + down_sum).astype(jnp.bfloat16)


def layer(queries, keys, values, out_weight):
    tok_rows, width = queries.shape
    half_sum = SUMMARY // 2
    my_index = lax.axis_index(CTX)
    rim_keys, rim_values = shifted((keys[tok_rows - BAND :], values[tok_rows - BAND :]), CTX, 1)
    band_keys = jnp.concatenate([rim_keys, keys], axis=0)
    band_values = jnp.concatenate([rim_values, values], axis=0)
    own_pos = my_index * tok_rows + jnp.arange(tok_rows, dtype=jnp.int32)
    band_pos = my_index * tok_rows - BAND + jnp.arange(tok_rows + BAND, dtype=jnp.int32)
    band_gap = own_pos[:, None] - band_pos[None, :]
    band_mask = (band_gap >= 0) & (band_gap < BAND) & (band_pos[None, :] >= 0)
    chunk = tok_rows // QUERY_CHUNKS
    near = [
        attend(queries[low : low + chunk], band_keys, band_values, band_mask[low : low + chunk])
        for low in range(0, tok_rows, chunk)
    ]
    core = lax.axis_index(CORE)
    sum_start = jnp.where(my_index % 2 == 0, tok_rows - half_sum, 0).astype(jnp.int32)
    own_keys = lax.dynamic_slice_in_dim(keys, sum_start, half_sum, 0)
    own_values = lax.dynamic_slice_in_dim(values, sum_start, half_sum, 0)
    chip_rows = lax.all_gather(
        jnp.concatenate([own_keys, own_values], axis=1), CORE, axis=0, tiled=True
    )
    my_half = lax.dynamic_slice_in_dim(chip_rows, core * width, width, 1)
    gathered = lax.all_gather(my_half, "cy", axis=0, tiled=True)
    gathered, offsets = gather_row_blocks(gathered, "cx")
    other = lax.ppermute(gathered, CORE, [(0, 1), (1, 0)])
    both = jnp.stack([gathered, other])
    all_sum_keys = both[core]
    all_sum_values = both[1 - core]
    index = jnp.arange(all_sum_keys.shape[0], dtype=jnp.int32)
    row_len = index.shape[0] // len(offsets)
    x_count = lax.axis_size("cx")
    moved = jnp.asarray(offsets, jnp.int32)[index // row_len]
    source_x = (lax.axis_index("cx") + moved) % x_count
    owner = source_x * (row_len // half_sum) + (index % row_len) // half_sum
    key_pos = (
        owner * tok_rows + jnp.where(owner % 2 == 0, tok_rows - half_sum, 0) + index % half_sum
    )
    sum_mask = own_pos[:, None] - key_pos[None, :] >= BAND
    pieces = []
    for low in range(0, tok_rows, chunk):
        rows = slice(low, low + chunk)
        far = attend(queries[rows], all_sum_keys, all_sum_values, sum_mask[rows])
        merged = combine_terms(near[low // chunk], far)
        pieces.append(merged[2] / merged[1][:, :, None])
    heads_out = jnp.concatenate(pieces, axis=1)
    attn = jnp.transpose(heads_out, (1, 0, 2)).reshape(tok_rows, width).astype(jnp.bfloat16)
    partial = jnp.dot(attn, out_weight, preferred_element_type=jnp.float32)
    return ring_reduce_scatter(partial, "head")


def solution(mesh):
    ctx_size, head_size = mesh.devices.shape
    split = mesh.devices.reshape(ctx_size // 16, 8, 2, head_size)
    fine = Mesh(split, ("cx", "cy", "cc", "head"))
    placed = (P(CTX, "head"), P(CTX, "head"), P(CTX, "head"), P("head", None))
    return jax.shard_map(
        layer, mesh=fine, in_specs=placed, out_specs=P(CTX + ("head",), None), check_vma=False
    )
```

```python
import math

import jax
import jax.numpy as jnp
from jax import lax
from jax.sharding import Mesh, PartitionSpec as P

HEAD_DIM = 128
BAND = 256
SUMMARY = 128
CTX = ("cx", "cy", "cc")
CORE = "cc"
QUERY_CHUNKS = 1


LOW_SCORE = -1e30


def shifted(value, axis, steps):
    count = lax.axis_size(axis)
    leading, last = (max(0, -steps), min(count, count - steps))
    return lax.ppermute(value, axis, [(source, source + steps) for source in range(leading, last)])


def combine_terms(first, second):
    top_score = jnp.maximum(first[0], second[0])
    first_factor = jnp.exp(first[0] - top_score)
    second_factor = jnp.exp(second[0] - top_score)
    totals = first[1] * first_factor + second[1] * second_factor
    weighted = first[2] * first_factor[:, :, None] + second[2] * second_factor[:, :, None]
    return (top_score, totals, weighted)


def attend(query_rows, keys, values, allowed):
    scale = 1.0 / math.sqrt(HEAD_DIM)
    rows, width = query_rows.shape
    heads = width // HEAD_DIM
    q = query_rows.reshape(rows, heads, HEAD_DIM)
    k = keys.reshape(keys.shape[0], heads, HEAD_DIM)
    s = jnp.einsum("qhd,khd->hqk", q, k, preferred_element_type=jnp.float32) * scale
    s = jnp.where(allowed[None], s, LOW_SCORE)
    top = s.max(axis=2)
    w = jnp.where(allowed[None], jnp.exp(s - top[:, :, None]), 0.0)
    v = values.reshape(values.shape[0], heads, HEAD_DIM)
    summed = jnp.einsum(
        "hqk,khd->hqd", w.astype(jnp.bfloat16), v, preferred_element_type=jnp.float32
    )
    return top, w.sum(axis=2), summed


def gather_row_blocks(block, axis):
    count = lax.axis_size(axis)
    if count != 4:
        gathered = lax.all_gather(block, axis, axis=0, tiled=True)
        me = lax.axis_index(axis)
        return gathered, [(j - me) for j in range(count)]
    ahead = [(j, (j + 1) % count) for j in range(count)]
    behind = [(j, (j - 1) % count) for j in range(count)]
    from_left = lax.ppermute(block, axis, ahead)
    from_right = lax.ppermute(block, axis, behind)
    half = block.shape[0] // 2
    far = jnp.concatenate(
        [
            lax.ppermute(from_left[:half], axis, ahead),
            lax.ppermute(from_right[half:], axis, behind),
        ],
        axis=0,
    )
    return jnp.concatenate([block, from_left, far, from_right], axis=0), [0, -1, -2, 1]


def ring_reduce_scatter(partial, axis):
    count = lax.axis_size(axis)
    me = lax.axis_index(axis)
    rows = partial.shape[0] // count
    left_hops = count // 2
    right_hops = count - 1 - left_hops
    ahead = [(source, (source + 1) % count) for source in range(count)]
    behind = [(source, (source - 1) % count) for source in range(count)]

    def piece(block):
        return lax.dynamic_slice_in_dim(partial, (block % count) * rows, rows, 0)

    up = piece(me + left_hops).astype(jnp.bfloat16)
    down = piece(me - right_hops).astype(jnp.bfloat16)
    up_sum = down_sum = None
    for step in range(left_hops):
        up_sum = lax.ppermute(up, axis, ahead).astype(jnp.float32) + piece(
            me + left_hops - 1 - step
        )
        up = up_sum.astype(jnp.bfloat16)
        if step < right_hops:
            down_sum = lax.ppermute(down, axis, behind).astype(jnp.float32)
            if step < right_hops - 1:
                down_sum = down_sum + piece(me - right_hops + 1 + step)
                down = down_sum.astype(jnp.bfloat16)
    return (up_sum + down_sum).astype(jnp.bfloat16)


def layer(queries, keys, values, out_weight):
    tok_rows, width = queries.shape
    half_sum = SUMMARY // 2
    my_index = lax.axis_index(CTX)
    rim_keys, rim_values = shifted((keys[tok_rows - BAND :], values[tok_rows - BAND :]), CTX, 1)
    band_keys = jnp.concatenate([rim_keys, keys], axis=0)
    band_values = jnp.concatenate([rim_values, values], axis=0)
    own_pos = my_index * tok_rows + jnp.arange(tok_rows, dtype=jnp.int32)
    band_pos = my_index * tok_rows - BAND + jnp.arange(tok_rows + BAND, dtype=jnp.int32)
    band_gap = own_pos[:, None] - band_pos[None, :]
    band_mask = (band_gap >= 0) & (band_gap < BAND) & (band_pos[None, :] >= 0)
    chunk = tok_rows // QUERY_CHUNKS
    near = [
        attend(queries[low : low + chunk], band_keys, band_values, band_mask[low : low + chunk])
        for low in range(0, tok_rows, chunk)
    ]
    core = lax.axis_index(CORE)
    sum_start = jnp.where(my_index % 2 == 0, tok_rows - half_sum, 0).astype(jnp.int32)
    own_keys = lax.dynamic_slice_in_dim(keys, sum_start, half_sum, 0)
    own_values = lax.dynamic_slice_in_dim(values, sum_start, half_sum, 0)
    own_rows = jnp.concatenate([own_keys, own_values], axis=1)
    packed_q = queries.reshape(-1, own_rows.shape[1])
    per_core = own_rows.shape[0] + packed_q.shape[0]
    pair = lax.all_gather(jnp.concatenate([own_rows, packed_q], axis=0), CORE, axis=0, tiled=True)
    chip_rows = jnp.concatenate(
        [pair[: own_rows.shape[0]], pair[per_core : per_core + own_rows.shape[0]]], axis=0
    )
    partner_all = lax.dynamic_slice_in_dim(
        pair, (1 - core) * per_core + own_rows.shape[0], packed_q.shape[0], 0
    ).reshape(queries.shape)
    hd = HEAD_DIM
    swap = [(0, 1), (1, 0)]

    def cols(array, low):
        return lax.dynamic_slice_in_dim(array, low, hd, 1)

    my_half = jnp.concatenate([cols(chip_rows, core * hd), cols(chip_rows, width + core * hd)], axis=1)
    partner_q = cols(partner_all, core * hd)
    gathered = lax.all_gather(my_half, "cy", axis=0, tiled=True)
    gathered, offsets = gather_row_blocks(gathered, "cx")
    index = jnp.arange(gathered.shape[0], dtype=jnp.int32)
    row_len = index.shape[0] // len(offsets)
    x_count = lax.axis_size("cx")
    moved = jnp.asarray(offsets, jnp.int32)[index // row_len]
    source_x = (lax.axis_index("cx") + moved) % x_count
    owner = source_x * (row_len // half_sum) + (index % row_len) // half_sum
    key_pos = (
        owner * tok_rows + jnp.where(owner % 2 == 0, tok_rows - half_sum, 0) + index % half_sum
    )
    partner_pos = (my_index + 1 - 2 * core) * tok_rows + jnp.arange(tok_rows, dtype=jnp.int32)
    both_pos = jnp.concatenate([own_pos, partner_pos])
    sum_mask = both_pos[:, None] - key_pos[None, :] >= BAND
    q_both = jnp.concatenate([cols(queries, core * hd), partner_q], axis=0)
    top, total, summed = attend(q_both, gathered[:, :hd], gathered[:, hd:], sum_mask)
    mine = (top[:, :tok_rows], total[:, :tok_rows], summed[:, :tok_rows])
    packed = jnp.concatenate(
        [summed[0, tok_rows:], top[0, tok_rows:, None], total[0, tok_rows:, None]], axis=1
    )
    got = lax.ppermute(packed, CORE, swap)
    theirs = (got[None, :, hd], got[None, :, hd + 1], got[None, :, :hd])
    first = core == 0
    far = tuple(
        jnp.concatenate([jnp.where(first, a, b), jnp.where(first, b, a)], axis=0)
        for a, b in zip(mine, theirs)
    )
    merged = combine_terms(near[0], far)
    heads_out = merged[2] / merged[1][:, :, None]
    attn = jnp.transpose(heads_out, (1, 0, 2)).reshape(tok_rows, width).astype(jnp.bfloat16)
    partial = jnp.dot(attn, out_weight, preferred_element_type=jnp.float32)
    return ring_reduce_scatter(partial, "head")


def solution(mesh):
    ctx_size, head_size = mesh.devices.shape
    split = mesh.devices.reshape(ctx_size // 16, 8, 2, head_size)
    fine = Mesh(split, ("cx", "cy", "cc", "head"))
    placed = (P(CTX, "head"), P(CTX, "head"), P(CTX, "head"), P("head", None))
    return jax.shard_map(
        layer, mesh=fine, in_specs=placed, out_specs=P(CTX + ("head",), None), check_vma=False
    )
```

```python
import math

import jax
import jax.numpy as jnp
from jax import lax
from jax.sharding import Mesh, PartitionSpec as P

HEAD_DIM = 128
BAND = 256
SUMMARY = 128
CTX = ("cx", "cy", "cc")
CORE = "cc"
QUERY_CHUNKS = 1


LOW_SCORE = -1e30


def shifted(value, axis, steps):
    count = lax.axis_size(axis)
    leading, last = (max(0, -steps), min(count, count - steps))
    return lax.ppermute(value, axis, [(source, source + steps) for source in range(leading, last)])


def combine_terms(first, second):
    top_score = jnp.maximum(first[0], second[0])
    first_factor = jnp.exp(first[0] - top_score)
    second_factor = jnp.exp(second[0] - top_score)
    totals = first[1] * first_factor + second[1] * second_factor
    weighted = first[2] * first_factor[:, :, None] + second[2] * second_factor[:, :, None]
    return (top_score, totals, weighted)


def attend(query_rows, keys, values, allowed):
    scale = 1.0 / math.sqrt(HEAD_DIM)
    rows, width = query_rows.shape
    heads = width // HEAD_DIM
    q = query_rows.reshape(rows, heads, HEAD_DIM)
    k = keys.reshape(keys.shape[0], heads, HEAD_DIM)
    s = jnp.einsum("qhd,khd->hqk", q, k, preferred_element_type=jnp.float32) * scale
    s = jnp.where(allowed[None], s, LOW_SCORE)
    top = s.max(axis=2)
    w = jnp.where(allowed[None], jnp.exp(s - top[:, :, None]), 0.0)
    v = values.reshape(values.shape[0], heads, HEAD_DIM)
    summed = jnp.einsum(
        "hqk,khd->hqd", w.astype(jnp.bfloat16), v, preferred_element_type=jnp.float32
    )
    return top, w.sum(axis=2), summed


def gather_row_blocks(block, axis):
    count = lax.axis_size(axis)
    if count != 4:
        gathered = lax.all_gather(block, axis, axis=0, tiled=True)
        me = lax.axis_index(axis)
        return gathered, [(j - me) for j in range(count)]
    ahead = [(j, (j + 1) % count) for j in range(count)]
    behind = [(j, (j - 1) % count) for j in range(count)]
    from_left = lax.ppermute(block, axis, ahead)
    from_right = lax.ppermute(block, axis, behind)
    half = block.shape[0] // 2
    far = jnp.concatenate(
        [
            lax.ppermute(from_left[:half], axis, ahead),
            lax.ppermute(from_right[half:], axis, behind),
        ],
        axis=0,
    )
    return jnp.concatenate([block, from_left, far, from_right], axis=0), [0, -1, -2, 1]


def ring_reduce_scatter(partial, axis):
    count = lax.axis_size(axis)
    me = lax.axis_index(axis)
    rows = partial.shape[0] // count
    left_hops = count // 2
    right_hops = count - 1 - left_hops
    ahead = [(source, (source + 1) % count) for source in range(count)]
    behind = [(source, (source - 1) % count) for source in range(count)]

    def piece(block):
        return lax.dynamic_slice_in_dim(partial, (block % count) * rows, rows, 0)

    up = piece(me + left_hops).astype(jnp.bfloat16)
    down = piece(me - right_hops).astype(jnp.bfloat16)
    up_sum = down_sum = None
    for step in range(left_hops):
        up_sum = lax.ppermute(up, axis, ahead).astype(jnp.float32) + piece(
            me + left_hops - 1 - step
        )
        up = up_sum.astype(jnp.bfloat16)
        if step < right_hops:
            down_sum = lax.ppermute(down, axis, behind).astype(jnp.float32)
            if step < right_hops - 1:
                down_sum = down_sum + piece(me - right_hops + 1 + step)
                down = down_sum.astype(jnp.bfloat16)
    return (up_sum + down_sum).astype(jnp.bfloat16)


def layer(queries, keys, values, out_weight):
    tok_rows, width = queries.shape
    half_sum = SUMMARY // 2
    my_index = lax.axis_index(CTX)
    rim = shifted(
        jnp.concatenate([keys[tok_rows - BAND :], values[tok_rows - BAND :]], axis=1), CTX, 1
    )
    rim_keys, rim_values = rim[:, :width], rim[:, width:]
    band_keys = jnp.concatenate([rim_keys, keys], axis=0)
    band_values = jnp.concatenate([rim_values, values], axis=0)
    own_pos = my_index * tok_rows + jnp.arange(tok_rows, dtype=jnp.int32)
    band_pos = my_index * tok_rows - BAND + jnp.arange(tok_rows + BAND, dtype=jnp.int32)
    band_gap = own_pos[:, None] - band_pos[None, :]
    band_mask = (band_gap >= 0) & (band_gap < BAND) & (band_pos[None, :] >= 0)
    chunk = tok_rows // QUERY_CHUNKS
    near = [
        attend(queries[low : low + chunk], band_keys, band_values, band_mask[low : low + chunk])
        for low in range(0, tok_rows, chunk)
    ]
    core = lax.axis_index(CORE)
    sum_start = jnp.where(my_index % 2 == 0, tok_rows - half_sum, 0).astype(jnp.int32)
    own_keys = lax.dynamic_slice_in_dim(keys, sum_start, half_sum, 0)
    own_values = lax.dynamic_slice_in_dim(values, sum_start, half_sum, 0)
    chip_rows = lax.all_gather(
        jnp.concatenate([own_keys, own_values], axis=1), CORE, axis=0, tiled=True
    )
    hd = HEAD_DIM
    swap = [(0, 1), (1, 0)]

    def cols(array, low):
        return lax.dynamic_slice_in_dim(array, low, hd, 1)

    my_half = jnp.concatenate([cols(chip_rows, core * hd), cols(chip_rows, width + core * hd)], axis=1)
    partner_q = lax.ppermute(cols(queries, (1 - core) * hd), CORE, swap)
    gathered = lax.all_gather(my_half, "cy", axis=0, tiled=True)
    gathered, offsets = gather_row_blocks(gathered, "cx")
    index = jnp.arange(gathered.shape[0], dtype=jnp.int32)
    row_len = index.shape[0] // len(offsets)
    x_count = lax.axis_size("cx")
    moved = jnp.asarray(offsets, jnp.int32)[index // row_len]
    source_x = (lax.axis_index("cx") + moved) % x_count
    owner = source_x * (row_len // half_sum) + (index % row_len) // half_sum
    key_pos = (
        owner * tok_rows + jnp.where(owner % 2 == 0, tok_rows - half_sum, 0) + index % half_sum
    )
    partner_pos = (my_index + 1 - 2 * core) * tok_rows + jnp.arange(tok_rows, dtype=jnp.int32)
    both_pos = jnp.concatenate([own_pos, partner_pos])
    sum_mask = both_pos[:, None] - key_pos[None, :] >= BAND
    q_both = jnp.concatenate([cols(queries, core * hd), partner_q], axis=0)
    top, total, summed = attend(q_both, gathered[:, :hd], gathered[:, hd:], sum_mask)
    mine = (top[:, :tok_rows], total[:, :tok_rows], summed[:, :tok_rows])
    packed = jnp.concatenate(
        [summed[0, tok_rows:], top[0, tok_rows:, None], total[0, tok_rows:, None]], axis=1
    )
    got = lax.ppermute(packed, CORE, swap)
    theirs = (got[None, :, hd], got[None, :, hd + 1], got[None, :, :hd])
    first = core == 0
    far = tuple(
        jnp.concatenate([jnp.where(first, a, b), jnp.where(first, b, a)], axis=0)
        for a, b in zip(mine, theirs)
    )
    merged = combine_terms(near[0], far)
    heads_out = merged[2] / merged[1][:, :, None]
    attn = jnp.transpose(heads_out, (1, 0, 2)).reshape(tok_rows, width).astype(jnp.bfloat16)
    partial = jnp.dot(attn, out_weight, preferred_element_type=jnp.float32)
    return ring_reduce_scatter(partial, "head")


def solution(mesh):
    ctx_size, head_size = mesh.devices.shape
    split = mesh.devices.reshape(ctx_size // 16, 8, 2, head_size)
    fine = Mesh(split, ("cx", "cy", "cc", "head"))
    placed = (P(CTX, "head"), P(CTX, "head"), P(CTX, "head"), P("head", None))
    return jax.shard_map(
        layer, mesh=fine, in_specs=placed, out_specs=P(CTX + ("head",), None), check_vma=False
    )
```

```python
import math

import jax
import jax.numpy as jnp
from jax import lax
from jax.sharding import Mesh, PartitionSpec as P

HEAD_DIM = 128
BAND = 256
SUMMARY = 128
CTX = ("cx", "cy", "cc")
CORE = "cc"
QUERY_CHUNKS = 1


LOW_SCORE = -1e30


def shifted(value, axis, steps):
    count = lax.axis_size(axis)
    leading, last = (max(0, -steps), min(count, count - steps))
    return lax.ppermute(value, axis, [(source, source + steps) for source in range(leading, last)])


def combine_terms(first, second):
    top_score = jnp.maximum(first[0], second[0])
    first_factor = jnp.exp(first[0] - top_score)
    second_factor = jnp.exp(second[0] - top_score)
    totals = first[1] * first_factor + second[1] * second_factor
    weighted = first[2] * first_factor[:, :, None] + second[2] * second_factor[:, :, None]
    return (top_score, totals, weighted)


def attend(query_rows, keys, values, allowed):
    scale = 1.0 / math.sqrt(HEAD_DIM)
    rows, width = query_rows.shape
    heads = width // HEAD_DIM
    q = query_rows.reshape(rows, heads, HEAD_DIM)
    k = keys.reshape(keys.shape[0], heads, HEAD_DIM)
    s = jnp.einsum("qhd,khd->hqk", q, k, preferred_element_type=jnp.float32) * scale
    s = jnp.where(allowed[None], s, LOW_SCORE)
    top = s.max(axis=2)
    w = jnp.where(allowed[None], jnp.exp(s - top[:, :, None]), 0.0)
    v = values.reshape(values.shape[0], heads, HEAD_DIM)
    summed = jnp.einsum(
        "hqk,khd->hqd", w.astype(jnp.bfloat16), v, preferred_element_type=jnp.float32
    )
    return top, w.sum(axis=2), summed


def gather_row_blocks(block, axis):
    count = lax.axis_size(axis)
    if count != 4:
        gathered = lax.all_gather(block, axis, axis=0, tiled=True)
        me = lax.axis_index(axis)
        return gathered, [(j - me) for j in range(count)]
    ahead = [(j, (j + 1) % count) for j in range(count)]
    behind = [(j, (j - 1) % count) for j in range(count)]
    from_left = lax.ppermute(block, axis, ahead)
    from_right = lax.ppermute(block, axis, behind)
    half = block.shape[0] // 2
    far = jnp.concatenate(
        [
            lax.ppermute(from_left[:half], axis, ahead),
            lax.ppermute(from_right[half:], axis, behind),
        ],
        axis=0,
    )
    return jnp.concatenate([block, from_left, far, from_right], axis=0), [0, -1, -2, 1]


def ring_reduce_scatter(partial, axis):
    count = lax.axis_size(axis)
    me = lax.axis_index(axis)
    rows = partial.shape[0] // count
    left_hops = count // 2
    right_hops = count - 1 - left_hops
    ahead = [(source, (source + 1) % count) for source in range(count)]
    behind = [(source, (source - 1) % count) for source in range(count)]

    def piece(block):
        return lax.dynamic_slice_in_dim(partial, (block % count) * rows, rows, 0)

    up = piece(me + left_hops).astype(jnp.bfloat16)
    down = piece(me - right_hops).astype(jnp.bfloat16)
    up_sum = down_sum = None
    for step in range(left_hops):
        up_sum = lax.ppermute(up, axis, ahead).astype(jnp.float32) + piece(
            me + left_hops - 1 - step
        )
        up = up_sum.astype(jnp.bfloat16)
        if step < right_hops:
            down_sum = lax.ppermute(down, axis, behind).astype(jnp.float32)
            if step < right_hops - 1:
                down_sum = down_sum + piece(me - right_hops + 1 + step)
                down = down_sum.astype(jnp.bfloat16)
    return (up_sum + down_sum).astype(jnp.bfloat16)


def layer(queries, keys, values, out_weight):
    tok_rows, width = queries.shape
    half_sum = SUMMARY // 2
    my_index = lax.axis_index(CTX)
    rim_keys, rim_values = shifted((keys[tok_rows - BAND :], values[tok_rows - BAND :]), CTX, 1)
    band_keys = jnp.concatenate([rim_keys, keys], axis=0)
    band_values = jnp.concatenate([rim_values, values], axis=0)
    own_pos = my_index * tok_rows + jnp.arange(tok_rows, dtype=jnp.int32)
    band_pos = my_index * tok_rows - BAND + jnp.arange(tok_rows + BAND, dtype=jnp.int32)
    band_gap = own_pos[:, None] - band_pos[None, :]
    band_mask = (band_gap >= 0) & (band_gap < BAND) & (band_pos[None, :] >= 0)
    chunk = tok_rows // QUERY_CHUNKS
    near = [
        attend(queries[low : low + chunk], band_keys, band_values, band_mask[low : low + chunk])
        for low in range(0, tok_rows, chunk)
    ]
    core = lax.axis_index(CORE)
    sum_start = jnp.where(my_index % 2 == 0, tok_rows - half_sum, 0).astype(jnp.int32)
    own_keys = lax.dynamic_slice_in_dim(keys, sum_start, half_sum, 0)
    own_values = lax.dynamic_slice_in_dim(values, sum_start, half_sum, 0)
    chip_rows = lax.all_gather(
        jnp.concatenate([own_keys, own_values], axis=1), CORE, axis=0, tiled=True
    )
    hd = HEAD_DIM
    swap = [(0, 1), (1, 0)]

    def cols(array, low):
        return lax.dynamic_slice_in_dim(array, low, hd, 1)

    my_half = jnp.concatenate([cols(chip_rows, core * hd), cols(chip_rows, width + core * hd)], axis=1)
    partner_q = lax.ppermute(cols(queries, (1 - core) * hd), CORE, swap)
    gathered = lax.all_gather(my_half, "cy", axis=0, tiled=True)
    gathered, offsets = gather_row_blocks(gathered, "cx")
    index = jnp.arange(gathered.shape[0], dtype=jnp.int32)
    row_len = index.shape[0] // len(offsets)
    x_count = lax.axis_size("cx")
    moved = jnp.asarray(offsets, jnp.int32)[index // row_len]
    source_x = (lax.axis_index("cx") + moved) % x_count
    owner = source_x * (row_len // half_sum) + (index % row_len) // half_sum
    key_pos = (
        owner * tok_rows + jnp.where(owner % 2 == 0, tok_rows - half_sum, 0) + index % half_sum
    )
    partner_pos = (my_index + 1 - 2 * core) * tok_rows + jnp.arange(tok_rows, dtype=jnp.int32)
    both_pos = jnp.concatenate([own_pos, partner_pos])
    sum_mask = both_pos[:, None] - key_pos[None, :] >= BAND
    q_both = jnp.concatenate([cols(queries, core * hd), partner_q], axis=0)
    top, total, summed = attend(q_both, gathered[:, :hd], gathered[:, hd:], sum_mask)
    mine = (top[:, :tok_rows], total[:, :tok_rows], summed[:, :tok_rows])
    packed = jnp.concatenate(
        [summed[0, tok_rows:], top[0, tok_rows:, None], total[0, tok_rows:, None]], axis=1
    )
    got = lax.ppermute(packed, CORE, swap)
    theirs = (got[None, :, hd], got[None, :, hd + 1], got[None, :, :hd])
    first = core == 0
    far = tuple(
        jnp.concatenate([jnp.where(first, a, b), jnp.where(first, b, a)], axis=0)
        for a, b in zip(mine, theirs)
    )
    merged = combine_terms(near[0], far)
    heads_out = merged[2] / merged[1][:, :, None]
    attn = jnp.transpose(heads_out, (1, 0, 2)).reshape(tok_rows, width).astype(jnp.bfloat16)
    partial = jnp.dot(attn, out_weight, preferred_element_type=jnp.float32).astype(jnp.bfloat16)
    return ring_reduce_scatter(partial, "head")


def solution(mesh):
    ctx_size, head_size = mesh.devices.shape
    split = mesh.devices.reshape(ctx_size // 16, 8, 2, head_size)
    fine = Mesh(split, ("cx", "cy", "cc", "head"))
    placed = (P(CTX, "head"), P(CTX, "head"), P(CTX, "head"), P("head", None))
    return jax.shard_map(
        layer, mesh=fine, in_specs=placed, out_specs=P(CTX + ("head",), None), check_vma=False
    )
```
